128 devices in a mesh: leaf: 16 (over x, y), col: 8 (over z, core).
Axes of the slice: x: 4, y: 4, z: 4, core: 2. Of those that a mesh axis runs over, the one named last changes fastest.
Arguments:
- right_side: float32 [31, 2560, 256], P(None, 'leaf'), may hold values from -6 to 6
- reciprocal_pivot_matrix: bfloat16 [31, 2560, 2560], P(None, 'col', 'leaf'), as said below
- panels: bfloat16 [98, 2560, 2560], P(None, 'leaf', 'col'), may hold values from -0.03125 to 0.03125
- parent: int32 [31], replicated, may hold values from 16 to 30, as said below
Outputs:
- solution: float32 [31, 2560, 256], P(None, 'leaf')
The draws below stay inside these ranges and needn't reach their ends.
Inputs may be any that keep to these rules, and one draw needn't show every extreme that they name: Supernodes 0 to 15 have parents among 16 to 23, 16 to 23 among 24 to 27, 24 to 27 among 28 and 29, 28 and 29 have parent 30, and entry 30 is 30 itself; each supernode of levels 1 to 4 is the parent of exactly two supernodes of the level below. `reciprocal_pivot_matrix`: each block is lower triangular with a positive diagonal.
All inputs are finite; a program needn't handle non-finite values.
Results may differ from the reference program's by a relative error of at most 0.03.
Values may be sent and summed in bfloat16 or wider, within the bound.
No kernel may reach another device: no remote copies, remote signals or barrier semaphores. Data moves between devices by JAX's collectives and lax.ppermute only.
A program may use at most 192 MiB of HBM per device.

```python
import math
import jax
import jax.numpy as jnp
from jax import lax

B = 2560
NRHS = 256
NS = 31
NP = 98
N_LEAF = 16
N_COL = 8


def draw_reciprocal_pivot_matrix(key, part):
    lower_key = jax.random.fold_in(key, 11)
    diag_key = jax.random.fold_in(key, 12)
    row_index = lax.broadcasted_iota(jnp.int32, (NS, B, B), 1)
    columns = lax.broadcasted_iota(jnp.int32, (NS, B, B), 2)
    spread = jax.random.normal(lower_key, (NS, B, B), jnp.float32) * (0.5 / math.sqrt(B))
    scales = jax.random.uniform(diag_key, (NS, B, 1), jnp.float32, 0.5, 1.5)
    entries = jnp.where(columns < row_index, spread, jnp.where(columns == row_index, scales, 0.0))
    return entries.astype(jnp.bfloat16)


def draw_parent(key, part):
    division_count = []
    offset_node = 0
    for tree_level, node_count in enumerate((16, 8, 4, 2)):
        shuffled = jax.random.permutation(jax.random.fold_in(key, 21 + tree_level), node_count)
        division_count.append(offset_node + node_count + shuffled // 2)
        offset_node = offset_node + node_count
    division_count.append(jnp.full((1,), NS - 1, jnp.int32))
    return jnp.concatenate([piece.astype(jnp.int32) for piece in division_count])


def shard_levels(key, dims, pieces, low, largest):
    gain = 1.0
    for axis_at, parts in pieces:
        heights = jax.random.uniform(jax.random.fold_in(jax.random.fold_in(key, 6), axis_at), (parts,), jnp.float32, low / len(pieces), largest / len(pieces))
        gain = gain * jnp.repeat(jnp.exp(heights), dims[axis_at] // parts).reshape((-1,) + (1,) * (len(dims) - 1 - axis_at))
    return gain


def scatter_about(own_key, extent, scale, most, cuts=(), kind=jnp.bfloat16):
    drawn = jax.random.normal(own_key, extent, jnp.float32) * scale
    if len(cuts) > 0:
        drawn = shard_levels(own_key, extent, cuts, -0.22, 0.18) * drawn
    return jnp.clip(drawn, min=-most, max=most).astype(kind)


def setup_inputs(seed: int = 0) -> dict:
    key_of = jax.random.split(jax.random.key(seed), 5)
    right_side = scatter_about(key_of[0], (NS, B, NRHS), 1.0, 6.0, ((1, 16),), jnp.float32)
    reciprocal_pivot_matrix = draw_reciprocal_pivot_matrix(jax.random.fold_in(key_of[4], 71), 0)
    panels = scatter_about(key_of[2], (NP, B, B), (16 * B) ** -0.5, 0.03125, ((1, 16), (2, 8)))
    parent = draw_parent(jax.random.fold_in(key_of[4], 71), 0)
    return {"right_side": right_side, "reciprocal_pivot_matrix": reciprocal_pivot_matrix, "panels": panels, "parent": parent}


level_starts = (0, 16, 24, 28, 30)
level_counts = (16, 8, 4, 2, 1)


def pair_table():
    sources = []
    distances = []
    for tree_level in range(5):
        for tree_vertex in range(level_starts[tree_level], level_starts[tree_level] + level_counts[tree_level]):
            for distance in range(1, 5 - tree_level):
                sources.append(tree_vertex)
                distances.append(distance)
    return sources, distances


def node_level(tree_vertex):
    deepest = 0
    for tree_level in range(5):
        if level_starts[tree_level] <= tree_vertex:
            deepest = tree_level
    return deepest


def pair_ancestors(parent):
    sources, distances = pair_table()
    climbed = [jnp.arange(parent.shape[0], dtype=jnp.int32)]
    for distance in range(4):
        climbed.append(parent[climbed[-1]])
    return jnp.stack([climbed[distance][source_node] for source_node, distance in zip(sources, distances)]).astype(jnp.int32)


def rounded(values):
    return lax.optimization_barrier(values.astype(jnp.bfloat16)).astype(jnp.float32)


def reference(right_side, reciprocal_pivot_matrix, panels, parent):
    sources, distances = pair_table()
    ancestor = pair_ancestors(parent)
    cluster_breadth = right_side.shape[1]
    load_vector_count = right_side.shape[2]
    bottom_frontal_tile = cluster_breadth // N_LEAF
    col_block = cluster_breadth // N_COL
    forward_full = {}
    forward_half = {}
    for tree_level in range(5):
        start_node = level_starts[tree_level]
        node_count = level_counts[tree_level]
        reduced = right_side[start_node:start_node + node_count]
        if tree_level > 0:
            waiting_updates = jnp.zeros((node_count, N_COL, cluster_breadth, load_vector_count), jnp.float32)
            slots = jnp.arange(node_count, dtype=jnp.int32) + start_node
            for node_pairing in range(len(sources)):
                if node_level(sources[node_pairing]) + distances[node_pairing] == tree_level:
                    onehot = (slots == ancestor[node_pairing]).astype(jnp.float32)
                    product = jnp.einsum("ajc,jcr->jar", panels[node_pairing].astype(jnp.float32).reshape(cluster_breadth, N_COL, col_block), forward_half[sources[node_pairing]].astype(jnp.float32).reshape(N_COL, col_block, load_vector_count))
                    waiting_updates = waiting_updates + onehot[:, None, None, None] * product[None]
            reduced = reduced - jnp.sum(rounded(waiting_updates), axis=1)
        reduced_portion = lax.optimization_barrier(reduced.astype(jnp.bfloat16))
        for initial_position in range(node_count):
            tree_vertex = start_node + initial_position
            division_count = jnp.einsum("cfw,fwx->fcx", reciprocal_pivot_matrix[tree_vertex].astype(jnp.float32).reshape(cluster_breadth, N_LEAF, bottom_frontal_tile), reduced_portion[initial_position].astype(jnp.float32).reshape(N_LEAF, bottom_frontal_tile, load_vector_count))
            forward_value = jnp.sum(rounded(division_count), axis=0)
            forward_full[tree_vertex] = forward_value
            forward_half[tree_vertex] = lax.optimization_barrier(forward_value.astype(jnp.bfloat16))
    solution_half = jnp.zeros((NS, cluster_breadth, load_vector_count), jnp.bfloat16)
    results = [None] * 5
    for tree_level in (4, 3, 2, 1, 0):
        start_node = level_starts[tree_level]
        node_count = level_counts[tree_level]
        outputs = []
        for initial_position in range(node_count):
            tree_vertex = start_node + initial_position
            corrected = forward_full[tree_vertex]
            if tree_level < 4:
                waiting_updates = jnp.zeros((N_LEAF, cluster_breadth, load_vector_count), jnp.float32)
                for node_pairing in range(len(sources)):
                    if sources[node_pairing] == tree_vertex:
                        upper_node = solution_half[ancestor[node_pairing]]
                        waiting_updates = waiting_updates + jnp.einsum("uwk,uwn->ukn", panels[node_pairing].astype(jnp.float32).reshape(N_LEAF, bottom_frontal_tile, cluster_breadth), upper_node.astype(jnp.float32).reshape(N_LEAF, bottom_frontal_tile, load_vector_count))
                corrected = corrected - jnp.sum(rounded(waiting_updates), axis=0)
            corrected_half = lax.optimization_barrier(corrected.astype(jnp.bfloat16))
            division_count = jnp.einsum("jca,jcr->jar", reciprocal_pivot_matrix[tree_vertex].astype(jnp.float32).reshape(N_COL, col_block, cluster_breadth), corrected_half.astype(jnp.float32).reshape(N_COL, col_block, load_vector_count))
            outputs.append(jnp.sum(rounded(division_count), axis=0))
        level_solution = jnp.stack(outputs)
        solution_half = solution_half.at[start_node:start_node + node_count].set(lax.optimization_barrier(level_solution.astype(jnp.bfloat16)))
        results[tree_level] = level_solution
    return jnp.concatenate(results, axis=0)
```

```python
import jax
import jax.numpy as jnp
import numpy as np
from jax import lax
from jax.sharding import PartitionSpec as P

level_starts = (0, 16, 24, 28, 30)
level_counts = (16, 8, 4, 2, 1)

LEAF_FACTORS = ((1, 4), (4, 4))
COL_FACTORS = ((1, 2), (2, 4))


def pair_offset(tree_level):
    initial_position = 0
    for lower in range(tree_level):
        initial_position = initial_position + level_counts[lower] * (4 - lower)
    return initial_position


def climb_table(parent):
    climbed = [jnp.arange(parent.shape[0], dtype=jnp.int32)]
    for distance in range(4):
        climbed.append(jnp.take(parent, climbed[-1]))
    return climbed


def level_onehot(climbed, source_level, distance):
    start, count = level_starts[source_level], level_counts[source_level]
    target = source_level + distance
    anc = climbed[distance][start : start + count]
    slots = jnp.arange(level_counts[target], dtype=jnp.int32) + level_starts[target]
    return (slots[:, None] == anc[None, :]).astype(jnp.float32)


def pair_slice(panel_local, source_level, distance):
    start = pair_offset(source_level) + distance - 1
    stride = 4 - source_level
    stop = pair_offset(source_level) + level_counts[source_level] * stride
    return panel_local[start:stop:stride]


def ring_perm(n, stride, size, shift):
    perm = []
    for i in range(n):
        g = (i // stride) % size
        perm.append((i, i + (((g + shift) % size) - g) * stride))
    return perm


def group_allreduce(x, axis, n, factors):
    shape = x.shape
    idx = lax.axis_index(axis)
    cur = x.reshape(-1)
    for stride, size in factors:
        g = (idx // stride) % size
        pieces = cur.reshape(size, -1)
        acc = lax.dynamic_index_in_dim(pieces, g, keepdims=False).astype(jnp.float32)
        for shift in range(1, size):
            send = lax.dynamic_index_in_dim(pieces, (g + shift) % size, keepdims=False)
            acc = acc + lax.ppermute(send, axis, ring_perm(n, stride, size, shift)).astype(jnp.float32)
        cur = acc.astype(jnp.bfloat16)
    for stride, size in reversed(factors):
        g = (idx // stride) % size
        got = [cur] + [lax.ppermute(cur, axis, ring_perm(n, stride, size, shift)) for shift in range(1, size)]
        ordered = jnp.stack([got[0]] + [got[size - t] for t in range(1, size)])
        cur = jnp.roll(ordered, g, axis=0).reshape(-1)
    return cur.reshape(shape)


def solve(right_side, diag_local, panel_local, parent):
    climbed = climb_table(parent)
    n_leaf = 16
    n_col = 8
    forward_levels = [None] * 5
    forward_half = [None] * 5
    for tree_level in range(5):
        start_node = level_starts[tree_level]
        node_count = level_counts[tree_level]
        reduced = right_side[start_node : start_node + node_count]
        if tree_level > 0:
            partial_value = None
            for source_level in range(tree_level):
                distance = tree_level - source_level
                products = jnp.einsum(
                    "sjv,svk->sjk",
                    pair_slice(panel_local, source_level, distance),
                    forward_half[source_level],
                    preferred_element_type=jnp.float32,
                )
                onehot = level_onehot(climbed, source_level, distance)
                term = jnp.einsum("ks,sjr->kjr", onehot, products, precision=lax.Precision.HIGHEST)
                partial_value = term if partial_value is None else partial_value + term
            reduced = reduced - group_allreduce(
                partial_value.astype(jnp.bfloat16), "col", n_col, COL_FACTORS
            ).astype(jnp.float32)
        division_count = jnp.einsum(
            "kcl,klr->kcr",
            diag_local[start_node : start_node + node_count],
            reduced.astype(jnp.bfloat16),
            preferred_element_type=jnp.float32,
        )
        forward_value = group_allreduce(
            division_count.astype(jnp.bfloat16), "leaf", n_leaf, LEAF_FACTORS
        )
        forward_levels[tree_level] = forward_value.astype(jnp.float32)
        forward_half[tree_level] = forward_value
    solution_half = [None] * 5
    results = [None] * 5
    for tree_level in (4, 3, 2, 1, 0):
        start_node = level_starts[tree_level]
        node_count = level_counts[tree_level]
        corrected = forward_levels[tree_level]
        if tree_level < 4:
            partial_value = None
            for distance in range(1, 5 - tree_level):
                onehot = level_onehot(climbed, tree_level, distance)
                upper_node = jnp.einsum(
                    "ks,kjr->sjr",
                    onehot,
                    solution_half[tree_level + distance].astype(jnp.float32),
                    precision=lax.Precision.HIGHEST,
                ).astype(jnp.bfloat16)
                term = jnp.einsum(
                    "boj,boh->bjh",
                    pair_slice(panel_local, tree_level, distance),
                    upper_node,
                    preferred_element_type=jnp.float32,
                )
                partial_value = term if partial_value is None else partial_value + term
            corrected = corrected - group_allreduce(
                partial_value.astype(jnp.bfloat16), "leaf", n_leaf, LEAF_FACTORS
            ).astype(jnp.float32)
        division_count = jnp.einsum(
            "kcl,kcr->klr",
            diag_local[start_node : start_node + node_count],
            corrected.astype(jnp.bfloat16),
            preferred_element_type=jnp.float32,
        )
        solution = group_allreduce(division_count.astype(jnp.bfloat16), "col", n_col, COL_FACTORS)
        results[tree_level] = solution.astype(jnp.float32)
        solution_half[tree_level] = solution
    return jnp.concatenate(results, axis=0)


def solution(mesh):
    return jax.shard_map(
        solve,
        mesh=mesh,
        in_specs=(P(None, "leaf", None), P(None, "col", "leaf"), P(None, "leaf", "col"), P()),
        out_specs=P(None, "leaf", None),
        check_vma=False,
    )
```

```python
import jax
import jax.numpy as jnp
import numpy as np
from jax import lax
from jax.sharding import PartitionSpec as P

level_starts = (0, 16, 24, 28, 30)
level_counts = (16, 8, 4, 2, 1)


def pair_offset(tree_level):
    initial_position = 0
    for lower in range(tree_level):
        initial_position = initial_position + level_counts[lower] * (4 - lower)
    return initial_position


def climb_table(parent):
    climbed = [jnp.arange(parent.shape[0], dtype=jnp.int32)]
    for distance in range(4):
        climbed.append(jnp.take(parent, climbed[-1]))
    return climbed


def level_onehot(climbed, source_level, distance):
    start, count = level_starts[source_level], level_counts[source_level]
    target = source_level + distance
    anc = climbed[distance][start : start + count]
    slots = jnp.arange(level_counts[target], dtype=jnp.int32) + level_starts[target]
    return (slots[:, None] == anc[None, :]).astype(jnp.float32)


def pair_slice(panel_local, source_level, distance):
    start = pair_offset(source_level) + distance - 1
    stride = 4 - source_level
    stop = pair_offset(source_level) + level_counts[source_level] * stride
    return panel_local[start:stop:stride]


def xor_perm(n, bit):
    return [(i, i ^ bit) for i in range(n)]


def group_allreduce(x, axis, n):
    if x.size * 2 >= (1 << 20):
        return lax.psum(x, axis)
    bit = 1
    while bit < n:
        x = (x.astype(jnp.float32) + lax.ppermute(x, axis, xor_perm(n, bit)).astype(jnp.float32)).astype(jnp.bfloat16)
        bit *= 2
    return x


def solve(right_side, diag_local, panel_local, parent):
    climbed = climb_table(parent)
    n_leaf = 16
    n_col = 8
    forward_levels = [None] * 5
    forward_half = [None] * 5
    for tree_level in range(5):
        start_node = level_starts[tree_level]
        node_count = level_counts[tree_level]
        reduced = right_side[start_node : start_node + node_count]
        if tree_level > 0:
            partial_value = None
            for source_level in range(tree_level):
                distance = tree_level - source_level
                products = jnp.einsum(
                    "sjv,svk->sjk",
                    pair_slice(panel_local, source_level, distance),
                    forward_half[source_level],
                    preferred_element_type=jnp.float32,
                )
                onehot = level_onehot(climbed, source_level, distance)
                term = jnp.einsum("ks,sjr->kjr", onehot, products, precision=lax.Precision.HIGHEST)
                partial_value = term if partial_value is None else partial_value + term
            reduced = reduced - group_allreduce(
                partial_value.astype(jnp.bfloat16), "col", n_col
            ).astype(jnp.float32)
        division_count = jnp.einsum(
            "kcl,klr->kcr",
            diag_local[start_node : start_node + node_count],
            reduced.astype(jnp.bfloat16),
            preferred_element_type=jnp.float32,
        )
        forward_value = group_allreduce(
            division_count.astype(jnp.bfloat16), "leaf", n_leaf
        )
        forward_levels[tree_level] = forward_value.astype(jnp.float32)
        forward_half[tree_level] = forward_value
    solution_half = [None] * 5
    results = [None] * 5
    for tree_level in (4, 3, 2, 1, 0):
        start_node = level_starts[tree_level]
        node_count = level_counts[tree_level]
        corrected = forward_levels[tree_level]
        if tree_level < 4:
            partial_value = None
            for distance in range(1, 5 - tree_level):
                onehot = level_onehot(climbed, tree_level, distance)
                upper_node = jnp.einsum(
                    "ks,kjr->sjr",
                    onehot,
                    solution_half[tree_level + distance].astype(jnp.float32),
                    precision=lax.Precision.HIGHEST,
                ).astype(jnp.bfloat16)
                term = jnp.einsum(
                    "boj,boh->bjh",
                    pair_slice(panel_local, tree_level, distance),
                    upper_node,
                    preferred_element_type=jnp.float32,
                )
                partial_value = term if partial_value is None else partial_value + term
            corrected = corrected - group_allreduce(
                partial_value.astype(jnp.bfloat16), "leaf", n_leaf
            ).astype(jnp.float32)
        division_count = jnp.einsum(
            "kcl,kcr->klr",
            diag_local[start_node : start_node + node_count],
            corrected.astype(jnp.bfloat16),
            preferred_element_type=jnp.float32,
        )
        solution = group_allreduce(division_count.astype(jnp.bfloat16), "col", n_col)
        results[tree_level] = solution.astype(jnp.float32)
        solution_half[tree_level] = solution
    return jnp.concatenate(results, axis=0)


def solution(mesh):
    return jax.shard_map(
        solve,
        mesh=mesh,
        in_specs=(P(None, "leaf", None), P(None, "col", "leaf"), P(None, "leaf", "col"), P()),
        out_specs=P(None, "leaf", None),
        check_vma=False,
    )
```

```python
import jax
import jax.numpy as jnp
import numpy as np
from jax import lax
from jax.sharding import PartitionSpec as P

level_starts = (0, 16, 24, 28, 30)
level_counts = (16, 8, 4, 2, 1)


def pair_offset(tree_level):
    initial_position = 0
    for lower in range(tree_level):
        initial_position = initial_position + level_counts[lower] * (4 - lower)
    return initial_position


def climb_table(parent):
    climbed = [jnp.arange(parent.shape[0], dtype=jnp.int32)]
    for distance in range(4):
        climbed.append(jnp.take(parent, climbed[-1]))
    return climbed


def level_onehot(climbed, source_level, distance):
    start, count = level_starts[source_level], level_counts[source_level]
    target = source_level + distance
    anc = climbed[distance][start : start + count]
    slots = jnp.arange(level_counts[target], dtype=jnp.int32) + level_starts[target]
    return (slots[:, None] == anc[None, :]).astype(jnp.float32)


def pair_slice(panel_local, source_level, distance):
    start = pair_offset(source_level) + distance - 1
    stride = 4 - source_level
    stop = pair_offset(source_level) + level_counts[source_level] * stride
    return panel_local[start:stop:stride]


def xor_perm(n, bit):
    return [(i, i ^ bit) for i in range(n)]


def a2a_allreduce(x, axis, n):
    shape = x.shape
    k = shape[0]
    if k >= n:
        pieces = x.reshape((n, k // n) + shape[1:])
    else:
        rows = shape[1] * k // n
        pieces = x.reshape((n, 1, rows) + shape[2:])
    got = lax.all_to_all(pieces, axis, 0, 0, tiled=False)
    owned = jnp.sum(got.astype(jnp.float32), axis=0).astype(jnp.bfloat16)
    spread = lax.all_to_all(jnp.broadcast_to(owned[None], (n,) + owned.shape), axis, 0, 0, tiled=False)
    return spread.reshape(shape)


def doubling_allreduce(x, axis, n):
    bit = 1
    while bit < n:
        x = (x.astype(jnp.float32) + lax.ppermute(x, axis, xor_perm(n, bit)).astype(jnp.float32)).astype(jnp.bfloat16)
        bit *= 2
    return x


def group_allreduce(x, axis, n):
    small = 1 if axis == "leaf" else 4
    if x.shape[0] <= small:
        return doubling_allreduce(x, axis, n)
    return a2a_allreduce(x, axis, n)


def solve(right_side, diag_local, panel_local, parent):
    climbed = climb_table(parent)
    n_leaf = 16
    n_col = 8
    forward_levels = [None] * 5
    forward_half = [None] * 5
    for tree_level in range(5):
        start_node = level_starts[tree_level]
        node_count = level_counts[tree_level]
        reduced = right_side[start_node : start_node + node_count]
        if tree_level > 0:
            partial_value = None
            for source_level in range(tree_level):
                distance = tree_level - source_level
                products = jnp.einsum(
                    "sjv,svk->sjk",
                    pair_slice(panel_local, source_level, distance),
                    forward_half[source_level],
                    preferred_element_type=jnp.float32,
                )
                onehot = level_onehot(climbed, source_level, distance)
                term = jnp.einsum("ks,sjr->kjr", onehot, products, precision=lax.Precision.HIGHEST)
                partial_value = term if partial_value is None else partial_value + term
            reduced = reduced - group_allreduce(
                partial_value.astype(jnp.bfloat16), "col", n_col
            ).astype(jnp.float32)
        division_count = jnp.einsum(
            "kcl,klr->kcr",
            diag_local[start_node : start_node + node_count],
            reduced.astype(jnp.bfloat16),
            preferred_element_type=jnp.float32,
        )
        forward_value = group_allreduce(
            division_count.astype(jnp.bfloat16), "leaf", n_leaf
        )
        forward_levels[tree_level] = forward_value.astype(jnp.float32)
        forward_half[tree_level] = forward_value
    solution_half = [None] * 5
    results = [None] * 5
    for tree_level in (4, 3, 2, 1, 0):
        start_node = level_starts[tree_level]
        node_count = level_counts[tree_level]
        corrected = forward_levels[tree_level]
        if tree_level < 4:
            partial_value = None
            for distance in range(1, 5 - tree_level):
                onehot = level_onehot(climbed, tree_level, distance)
                upper_node = jnp.einsum(
                    "ks,kjr->sjr",
                    onehot,
                    solution_half[tree_level + distance].astype(jnp.float32),
                    precision=lax.Precision.HIGHEST,
                ).astype(jnp.bfloat16)
                term = jnp.einsum(
                    "boj,boh->bjh",
                    pair_slice(panel_local, tree_level, distance),
                    upper_node,
                    preferred_element_type=jnp.float32,
                )
                partial_value = term if partial_value is None else partial_value + term
            corrected = corrected - group_allreduce(
                partial_value.astype(jnp.bfloat16), "leaf", n_leaf
            ).astype(jnp.float32)
        division_count = jnp.einsum(
            "kcl,kcr->klr",
            diag_local[start_node : start_node + node_count],
            corrected.astype(jnp.bfloat16),
            preferred_element_type=jnp.float32,
        )
        solution = group_allreduce(division_count.astype(jnp.bfloat16), "col", n_col)
        results[tree_level] = solution.astype(jnp.float32)
        solution_half[tree_level] = solution
    return jnp.concatenate(results, axis=0)


def solution(mesh):
    return jax.shard_map(
        solve,
        mesh=mesh,
        in_specs=(P(None, "leaf", None), P(None, "col", "leaf"), P(None, "leaf", "col"), P()),
        out_specs=P(None, "leaf", None),
        check_vma=False,
    )
```

```python
import jax
import jax.numpy as jnp
import numpy as np
from jax import lax
from jax.sharding import PartitionSpec as P

level_starts = (0, 16, 24, 28, 30)
level_counts = (16, 8, 4, 2, 1)


def pair_offset(tree_level):
    initial_position = 0
    for lower in range(tree_level):
        initial_position = initial_position + level_counts[lower] * (4 - lower)
    return initial_position


def climb_table(parent):
    climbed = [jnp.arange(parent.shape[0], dtype=jnp.int32)]
    for distance in range(4):
        climbed.append(jnp.take(parent, climbed[-1]))
    return climbed


def level_onehot(climbed, source_level, distance):
    start, count = level_starts[source_level], level_counts[source_level]
    target = source_level + distance
    anc = climbed[distance][start : start + count]
    slots = jnp.arange(level_counts[target], dtype=jnp.int32) + level_starts[target]
    return (slots[:, None] == anc[None, :]).astype(jnp.float32)


def pair_slice(panel_local, source_level, distance):
    start = pair_offset(source_level) + distance - 1
    stride = 4 - source_level
    stop = pair_offset(source_level) + level_counts[source_level] * stride
    return panel_local[start:stop:stride]


def xor_perm(n, bit):
    return [(i, i ^ bit) for i in range(n)]


def a2a_allreduce(x, axis, n):
    shape = x.shape
    k = shape[0]
    if k >= n:
        pieces = x.reshape((n, k // n) + shape[1:])
    else:
        rows = shape[1] * k // n
        pieces = x.reshape((n, 1, rows) + shape[2:])
    got = lax.all_to_all(pieces, axis, 0, 0, tiled=False)
    owned = jnp.sum(got.astype(jnp.float32), axis=0).astype(jnp.bfloat16)
    spread = lax.all_to_all(jnp.broadcast_to(owned[None], (n,) + owned.shape), axis, 0, 0, tiled=False)
    return spread.reshape(shape)


def doubling_allreduce(x, axis, n):
    bit = 1
    while bit < n:
        x = (x.astype(jnp.float32) + lax.ppermute(x, axis, xor_perm(n, bit)).astype(jnp.float32)).astype(jnp.bfloat16)
        bit *= 2
    return x


def group_allreduce(x, axis, n):
    small = 1 if axis == "leaf" else 4
    if x.shape[0] <= small:
        return doubling_allreduce(x, axis, n)
    return a2a_allreduce(x, axis, n)


def solve(right_side, diag_local, panel_local, parent):
    climbed = climb_table(parent)
    n_leaf = 16
    n_col = 8
    forward_levels = [None] * 5
    forward_half = [None] * 5
    for tree_level in range(5):
        start_node = level_starts[tree_level]
        node_count = level_counts[tree_level]
        reduced = right_side[start_node : start_node + node_count]
        if tree_level > 0:
            partial_value = None
            for source_level in range(tree_level):
                distance = tree_level - source_level
                products = jnp.einsum(
                    "sjv,svk->sjk",
                    pair_slice(panel_local, source_level, distance),
                    forward_half[source_level],
                    preferred_element_type=jnp.float32,
                )
                onehot = level_onehot(climbed, source_level, distance)
                term = jnp.einsum("ks,sjr->kjr", onehot, products, precision=lax.Precision.HIGHEST)
                partial_value = term if partial_value is None else partial_value + term
            reduced = reduced - group_allreduce(
                partial_value.astype(jnp.bfloat16), "col", n_col
            ).astype(jnp.float32)
        division_count = jnp.einsum(
            "kcl,klr->kcr",
            diag_local[start_node : start_node + node_count],
            reduced.astype(jnp.bfloat16),
            preferred_element_type=jnp.float32,
        )
        forward_value = group_allreduce(
            division_count.astype(jnp.bfloat16), "leaf", n_leaf
        )
        forward_levels[tree_level] = forward_value.astype(jnp.float32)
        forward_half[tree_level] = forward_value
    solution_half = [None] * 5
    results = [None] * 5
    for tree_level in (4, 3, 2, 1, 0):
        start_node = level_starts[tree_level]
        node_count = level_counts[tree_level]
        corrected = forward_levels[tree_level]
        if tree_level < 4:
            spread = 4 - tree_level
            first = pair_offset(tree_level)
            panel_block = panel_local[first : first + node_count * spread].reshape(
                (node_count, spread) + panel_local.shape[1:]
            )
            upper_node = jnp.stack(
                [
                    jnp.einsum(
                        "ks,kjr->sjr",
                        level_onehot(climbed, tree_level, distance),
                        solution_half[tree_level + distance].astype(jnp.float32),
                        precision=lax.Precision.HIGHEST,
                    )
                    for distance in range(1, spread + 1)
                ],
                axis=1,
            ).astype(jnp.bfloat16)
            partial_value = jnp.einsum(
                "sdoj,sdoh->sjh", panel_block, upper_node, preferred_element_type=jnp.float32
            )
            corrected = corrected - group_allreduce(
                partial_value.astype(jnp.bfloat16), "leaf", n_leaf
            ).astype(jnp.float32)
        division_count = jnp.einsum(
            "kcl,kcr->klr",
            diag_local[start_node : start_node + node_count],
            corrected.astype(jnp.bfloat16),
            preferred_element_type=jnp.float32,
        )
        solution = group_allreduce(division_count.astype(jnp.bfloat16), "col", n_col)
        results[tree_level] = solution.astype(jnp.float32)
        solution_half[tree_level] = solution
    return jnp.concatenate(results, axis=0)


def solution(mesh):
    return jax.shard_map(
        solve,
        mesh=mesh,
        in_specs=(P(None, "leaf", None), P(None, "col", "leaf"), P(None, "leaf", "col"), P()),
        out_specs=P(None, "leaf", None),
        check_vma=False,
    )
```

```python
import jax
import jax.numpy as jnp
import numpy as np
from jax import lax
from jax.sharding import PartitionSpec as P

level_starts = (0, 16, 24, 28, 30)
level_counts = (16, 8, 4, 2, 1)


def pair_offset(tree_level):
    initial_position = 0
    for lower in range(tree_level):
        initial_position = initial_position + level_counts[lower] * (4 - lower)
    return initial_position


def climb_table(parent):
    climbed = [jnp.arange(parent.shape[0], dtype=jnp.int32)]
    for distance in range(4):
        climbed.append(jnp.take(parent, climbed[-1]))
    return climbed


def level_onehot(climbed, source_level, distance):
    start, count = level_starts[source_level], level_counts[source_level]
    target = source_level + distance
    anc = climbed[distance][start : start + count]
    slots = jnp.arange(level_counts[target], dtype=jnp.int32) + level_starts[target]
    return (slots[:, None] == anc[None, :]).astype(jnp.float32)


def pair_slice(panel_local, source_level, distance):
    start = pair_offset(source_level) + distance - 1
    stride = 4 - source_level
    stop = pair_offset(source_level) + level_counts[source_level] * stride
    return panel_local[start:stop:stride]


def xor_perm(n, bit):
    return [(i, i ^ bit) for i in range(n)]


def a2a_allreduce(x, axis, n):
    shape = x.shape
    k = shape[0]
    if k >= n:
        pieces = x.reshape((n, k // n) + shape[1:])
    else:
        rows = shape[1] * k // n
        pieces = x.reshape((n, 1, rows) + shape[2:])
    got = lax.all_to_all(pieces, axis, 0, 0, tiled=False)
    owned = jnp.sum(got.astype(jnp.float32), axis=0).astype(jnp.bfloat16)
    spread = lax.all_to_all(jnp.broadcast_to(owned[None], (n,) + owned.shape), axis, 0, 0, tiled=False)
    return spread.reshape(shape)


def doubling_allreduce(x, axis, n):
    bit = 1
    while bit < n:
        x = (x.astype(jnp.float32) + lax.ppermute(x, axis, xor_perm(n, bit)).astype(jnp.float32)).astype(jnp.bfloat16)
        bit *= 2
    return x


def group_allreduce(x, axis, n):
    small = 1 if axis == "leaf" else 2
    if x.shape[0] <= small:
        return doubling_allreduce(x, axis, n)
    return a2a_allreduce(x, axis, n)


def solve(right_side, diag_local, panel_local, parent):
    climbed = climb_table(parent)
    n_leaf = 16
    n_col = 8
    forward_levels = [None] * 5
    forward_half = [None] * 5
    for tree_level in range(5):
        start_node = level_starts[tree_level]
        node_count = level_counts[tree_level]
        reduced = right_side[start_node : start_node + node_count]
        if tree_level > 0:
            partial_value = None
            for source_level in range(tree_level):
                distance = tree_level - source_level
                products = jnp.einsum(
                    "sjv,svk->sjk",
                    pair_slice(panel_local, source_level, distance),
                    forward_half[source_level],
                    preferred_element_type=jnp.float32,
                )
                onehot = level_onehot(climbed, source_level, distance)
                term = jnp.einsum("ks,sjr->kjr", onehot, products, precision=lax.Precision.HIGHEST)
                partial_value = term if partial_value is None else partial_value + term
            reduced = reduced - group_allreduce(
                partial_value.astype(jnp.bfloat16), "col", n_col
            ).astype(jnp.float32)
        division_count = jnp.einsum(
            "kcl,klr->kcr",
            diag_local[start_node : start_node + node_count],
            reduced.astype(jnp.bfloat16),
            preferred_element_type=jnp.float32,
        )
        forward_value = group_allreduce(
            division_count.astype(jnp.bfloat16), "leaf", n_leaf
        )
        forward_levels[tree_level] = forward_value.astype(jnp.float32)
        forward_half[tree_level] = forward_value
    solution_half = [None] * 5
    results = [None] * 5
    for tree_level in (4, 3, 2, 1, 0):
        start_node = level_starts[tree_level]
        node_count = level_counts[tree_level]
        corrected = forward_levels[tree_level]
        if tree_level < 4:
            partial_value = None
            for distance in range(1, 5 - tree_level):
                onehot = level_onehot(climbed, tree_level, distance)
                upper_node = jnp.einsum(
                    "ks,kjr->sjr",
                    onehot,
                    solution_half[tree_level + distance].astype(jnp.float32),
                    precision=lax.Precision.HIGHEST,
                ).astype(jnp.bfloat16)
                term = jnp.einsum(
                    "boj,boh->bjh",
                    pair_slice(panel_local, tree_level, distance),
                    upper_node,
                    preferred_element_type=jnp.float32,
                )
                partial_value = term if partial_value is None else partial_value + term
            corrected = corrected - group_allreduce(
                partial_value.astype(jnp.bfloat16), "leaf", n_leaf
            ).astype(jnp.float32)
        division_count = jnp.einsum(
            "kcl,kcr->klr",
            diag_local[start_node : start_node + node_count],
            corrected.astype(jnp.bfloat16),
            preferred_element_type=jnp.float32,
        )
        solution = group_allreduce(division_count.astype(jnp.bfloat16), "col", n_col)
        results[tree_level] = solution.astype(jnp.float32)
        solution_half[tree_level] = solution
    return jnp.concatenate(results, axis=0)


def solution(mesh):
    return jax.shard_map(
        solve,
        mesh=mesh,
        in_specs=(P(None, "leaf", None), P(None, "col", "leaf"), P(None, "leaf", "col"), P()),
        out_specs=P(None, "leaf", None),
        check_vma=False,
    )
```

```python
import jax
import jax.numpy as jnp
import numpy as np
from jax import lax
from jax.sharding import Mesh, PartitionSpec as P

level_starts = (0, 16, 24, 28, 30)
level_counts = (16, 8, 4, 2, 1)
LEAF = ("x", "y")
COL = ("z", "core")


def pair_offset(tree_level):
    initial_position = 0
    for lower in range(tree_level):
        initial_position = initial_position + level_counts[lower] * (4 - lower)
    return initial_position


def climb_table(parent):
    climbed = [jnp.arange(parent.shape[0], dtype=jnp.int32)]
    for distance in range(4):
        climbed.append(jnp.take(parent, climbed[-1]))
    return climbed


def level_onehot(climbed, source_level, distance):
    start, count = level_starts[source_level], level_counts[source_level]
    target = source_level + distance
    anc = climbed[distance][start : start + count]
    slots = jnp.arange(level_counts[target], dtype=jnp.int32) + level_starts[target]
    return (slots[:, None] == anc[None, :]).astype(jnp.float32)


def pair_slice(panel_local, source_level, distance):
    start = pair_offset(source_level) + distance - 1
    stride = 4 - source_level
    stop = pair_offset(source_level) + level_counts[source_level] * stride
    return panel_local[start:stop:stride]


def xor_perm(n, bit):
    return [(i, i ^ bit) for i in range(n)]


def a2a_allreduce(x, axis, n):
    shape = x.shape
    k = shape[0]
    if k >= n:
        pieces = x.reshape((n, k // n) + shape[1:])
    else:
        rows = shape[1] * k // n
        pieces = x.reshape((n, 1, rows) + shape[2:])
    got = lax.all_to_all(pieces, axis, 0, 0, tiled=False)
    owned = jnp.sum(got.astype(jnp.float32), axis=0).astype(jnp.bfloat16)
    spread = lax.all_to_all(jnp.broadcast_to(owned[None], (n,) + owned.shape), axis, 0, 0, tiled=False)
    return spread.reshape(shape)


def doubling_allreduce(x, axis, n):
    bit = 1
    while bit < n:
        x = (x.astype(jnp.float32) + lax.ppermute(x, axis, xor_perm(n, bit)).astype(jnp.float32)).astype(jnp.bfloat16)
        bit *= 2
    return x


def staged_allreduce(x, stages):
    shape = x.shape
    total = 1
    for _, size in stages:
        total *= size
    cur = x.reshape((total, shape[0] // total) + shape[1:])
    for axis, size in stages:
        pieces = cur.reshape((size, cur.shape[0] // size) + cur.shape[1:])
        got = lax.all_to_all(pieces, axis, 0, 0, tiled=False)
        cur = jnp.sum(got.astype(jnp.float32), axis=0).astype(jnp.bfloat16)
    for axis, size in reversed(stages):
        spread = lax.all_to_all(jnp.broadcast_to(cur[None], (size,) + cur.shape), axis, 0, 0, tiled=False)
        cur = spread.reshape((size * cur.shape[0],) + cur.shape[1:])
    return cur.reshape(shape)


def group_allreduce(x, axis, n):
    small = 1 if axis == LEAF else 4
    if x.shape[0] <= small:
        return doubling_allreduce(x, axis, n)
    if axis == COL and x.shape[0] >= 2 * n:
        return staged_allreduce(x, (("core", 2), ("z", 4)))
    return a2a_allreduce(x, axis, n)


def solve(right_side, diag_local, panel_local, parent):
    climbed = climb_table(parent)
    n_leaf = 16
    n_col = 8
    forward_levels = [None] * 5
    forward_half = [None] * 5
    for tree_level in range(5):
        start_node = level_starts[tree_level]
        node_count = level_counts[tree_level]
        reduced = right_side[start_node : start_node + node_count]
        if tree_level > 0:
            partial_value = None
            for source_level in range(tree_level):
                distance = tree_level - source_level
                products = jnp.einsum(
                    "sjv,svk->sjk",
                    pair_slice(panel_local, source_level, distance),
                    forward_half[source_level],
                    preferred_element_type=jnp.float32,
                )
                onehot = level_onehot(climbed, source_level, distance)
                term = jnp.einsum("ks,sjr->kjr", onehot, products, precision=lax.Precision.HIGHEST)
                partial_value = term if partial_value is None else partial_value + term
            reduced = reduced - group_allreduce(
                partial_value.astype(jnp.bfloat16), COL, n_col
            ).astype(jnp.float32)
        division_count = jnp.einsum(
            "kcl,klr->kcr",
            diag_local[start_node : start_node + node_count],
            reduced.astype(jnp.bfloat16),
            preferred_element_type=jnp.float32,
        )
        forward_value = group_allreduce(
            division_count.astype(jnp.bfloat16), LEAF, n_leaf
        )
        forward_levels[tree_level] = forward_value.astype(jnp.float32)
        forward_half[tree_level] = forward_value
    solution_half = [None] * 5
    results = [None] * 5
    for tree_level in (4, 3, 2, 1, 0):
        start_node = level_starts[tree_level]
        node_count = level_counts[tree_level]
        corrected = forward_levels[tree_level]
        if tree_level < 4:
            partial_value = None
            for distance in range(1, 5 - tree_level):
                onehot = level_onehot(climbed, tree_level, distance)
                upper_node = jnp.einsum(
                    "ks,kjr->sjr",
                    onehot,
                    solution_half[tree_level + distance].astype(jnp.float32),
                    precision=lax.Precision.HIGHEST,
                ).astype(jnp.bfloat16)
                term = jnp.einsum(
                    "boj,boh->bjh",
                    pair_slice(panel_local, tree_level, distance),
                    upper_node,
                    preferred_element_type=jnp.float32,
                )
                partial_value = term if partial_value is None else partial_value + term
            corrected = corrected - group_allreduce(
                partial_value.astype(jnp.bfloat16), LEAF, n_leaf
            ).astype(jnp.float32)
        division_count = jnp.einsum(
            "kcl,kcr->klr",
            diag_local[start_node : start_node + node_count],
            corrected.astype(jnp.bfloat16),
            preferred_element_type=jnp.float32,
        )
        solution = group_allreduce(division_count.astype(jnp.bfloat16), COL, n_col)
        results[tree_level] = solution.astype(jnp.float32)
        solution_half[tree_level] = solution
    return jnp.concatenate(results, axis=0)


def solution(mesh):
    chips = Mesh(mesh.devices.reshape(4, 4, 4, 2), ("x", "y", "z", "core"))
    return jax.shard_map(
        solve,
        mesh=chips,
        in_specs=(P(None, LEAF, None), P(None, COL, LEAF), P(None, LEAF, COL), P()),
        out_specs=P(None, LEAF, None),
        check_vma=False,
    )
```

```python
import jax
import jax.numpy as jnp
import numpy as np
from jax import lax
from jax.sharding import Mesh, PartitionSpec as P

level_starts = (0, 16, 24, 28, 30)
level_counts = (16, 8, 4, 2, 1)
LEAF = ("x", "y")
COL = ("z", "core")


def pair_offset(tree_level):
    initial_position = 0
    for lower in range(tree_level):
        initial_position = initial_position + level_counts[lower] * (4 - lower)
    return initial_position


def climb_table(parent):
    climbed = [jnp.arange(parent.shape[0], dtype=jnp.int32)]
    for distance in range(4):
        climbed.append(jnp.take(parent, climbed[-1]))
    return climbed


def level_onehot(climbed, source_level, distance):
    start, count = level_starts[source_level], level_counts[source_level]
    target = source_level + distance
    anc = climbed[distance][start : start + count]
    slots = jnp.arange(level_counts[target], dtype=jnp.int32) + level_starts[target]
    return (slots[:, None] == anc[None, :]).astype(jnp.float32)


def pair_slice(panel_local, source_level, distance):
    start = pair_offset(source_level) + distance - 1
    stride = 4 - source_level
    stop = pair_offset(source_level) + level_counts[source_level] * stride
    return panel_local[start:stop:stride]


def xor_perm(n, bit):
    return [(i, i ^ bit) for i in range(n)]


def a2a_allreduce(x, axis, n):
    shape = x.shape
    k = shape[0]
    if k >= n:
        pieces = x.reshape((n, k // n) + shape[1:])
    else:
        rows = shape[1] * k // n
        pieces = x.reshape((n, 1, rows) + shape[2:])
    got = lax.all_to_all(pieces, axis, 0, 0, tiled=False)
    owned = jnp.sum(got.astype(jnp.float32), axis=0).astype(jnp.bfloat16)
    spread = lax.all_to_all(jnp.broadcast_to(owned[None], (n,) + owned.shape), axis, 0, 0, tiled=False)
    return spread.reshape(shape)


def doubling_allreduce(x, axis, n):
    bit = 1
    while bit < n:
        x = (x.astype(jnp.float32) + lax.ppermute(x, axis, xor_perm(n, bit)).astype(jnp.float32)).astype(jnp.bfloat16)
        bit *= 2
    return x


def staged_allreduce(x, stages):
    shape = x.shape
    total = 1
    for _, size in stages:
        total *= size
    cur = x.reshape((total, shape[0] // total) + shape[1:])
    for axis, size in stages:
        pieces = cur.reshape((size, cur.shape[0] // size) + cur.shape[1:])
        got = lax.all_to_all(pieces, axis, 0, 0, tiled=False)
        cur = jnp.sum(got.astype(jnp.float32), axis=0).astype(jnp.bfloat16)
    for axis, size in reversed(stages):
        spread = lax.all_to_all(jnp.broadcast_to(cur[None], (size,) + cur.shape), axis, 0, 0, tiled=False)
        cur = spread.reshape((size * cur.shape[0],) + cur.shape[1:])
    return cur.reshape(shape)


def col_halved_allreduce(x):
    core = lax.axis_index("core")
    swap = [(0, 1), (1, 0)]
    halves = x.reshape((x.shape[0], 2, x.shape[1] // 2) + x.shape[2:])
    keep = lax.dynamic_index_in_dim(halves, core, axis=1, keepdims=False)
    send = lax.dynamic_index_in_dim(halves, 1 - core, axis=1, keepdims=False)
    acc = (keep.astype(jnp.float32) + lax.ppermute(send, "core", swap).astype(jnp.float32)).astype(jnp.bfloat16)
    acc = doubling_allreduce(acc, "z", 4)
    other = lax.ppermute(acc, "core", swap)
    low = jnp.where(core == 0, acc, other)
    high = jnp.where(core == 0, other, acc)
    return jnp.stack([low, high], axis=1).reshape(x.shape)


def group_allreduce(x, axis, n):
    small = 1 if axis == LEAF else 4
    if x.shape[0] <= small:
        if axis == COL:
            return col_halved_allreduce(x)
        return doubling_allreduce(x, axis, n)
    if axis == COL and x.shape[0] >= 2 * n:
        return staged_allreduce(x, (("core", 2), ("z", 4)))
    return a2a_allreduce(x, axis, n)


def solve(right_side, diag_local, panel_local, parent):
    climbed = climb_table(parent)
    n_leaf = 16
    n_col = 8
    forward_levels = [None] * 5
    forward_half = [None] * 5
    for tree_level in range(5):
        start_node = level_starts[tree_level]
        node_count = level_counts[tree_level]
        reduced = right_side[start_node : start_node + node_count]
        if tree_level > 0:
            partial_value = None
            for source_level in range(tree_level):
                distance = tree_level - source_level
                products = jnp.einsum(
                    "sjv,svk->sjk",
                    pair_slice(panel_local, source_level, distance),
                    forward_half[source_level],
                    preferred_element_type=jnp.float32,
                )
                onehot = level_onehot(climbed, source_level, distance)
                term = jnp.einsum("ks,sjr->kjr", onehot, products, precision=lax.Precision.HIGHEST)
                partial_value = term if partial_value is None else partial_value + term
            reduced = reduced - group_allreduce(
                partial_value.astype(jnp.bfloat16), COL, n_col
            ).astype(jnp.float32)
        division_count = jnp.einsum(
            "kcl,klr->kcr",
            diag_local[start_node : start_node + node_count],
            reduced.astype(jnp.bfloat16),
            preferred_element_type=jnp.float32,
        )
        forward_value = group_allreduce(
            division_count.astype(jnp.bfloat16), LEAF, n_leaf
        )
        forward_levels[tree_level] = forward_value.astype(jnp.float32)
        forward_half[tree_level] = forward_value
    solution_half = [None] * 5
    results = [None] * 5
    for tree_level in (4, 3, 2, 1, 0):
        start_node = level_starts[tree_level]
        node_count = level_counts[tree_level]
        corrected = forward_levels[tree_level]
        if tree_level < 4:
            partial_value = None
            for distance in range(1, 5 - tree_level):
                onehot = level_onehot(climbed, tree_level, distance)
                upper_node = jnp.einsum(
                    "ks,kjr->sjr",
                    onehot,
                    solution_half[tree_level + distance].astype(jnp.float32),
                    precision=lax.Precision.HIGHEST,
                ).astype(jnp.bfloat16)
                term = jnp.einsum(
                    "boj,boh->bjh",
                    pair_slice(panel_local, tree_level, distance),
                    upper_node,
                    preferred_element_type=jnp.float32,
                )
                partial_value = term if partial_value is None else partial_value + term
            corrected = corrected - group_allreduce(
                partial_value.astype(jnp.bfloat16), LEAF, n_leaf
            ).astype(jnp.float32)
        division_count = jnp.einsum(
            "kcl,kcr->klr",
            diag_local[start_node : start_node + node_count],
            corrected.astype(jnp.bfloat16),
            preferred_element_type=jnp.float32,
        )
        solution = group_allreduce(division_count.astype(jnp.bfloat16), COL, n_col)
        results[tree_level] = solution.astype(jnp.float32)
        solution_half[tree_level] = solution
    return jnp.concatenate(results, axis=0)


def solution(mesh):
    chips = Mesh(mesh.devices.reshape(4, 4, 4, 2), ("x", "y", "z", "core"))
    return jax.shard_map(
        solve,
        mesh=chips,
        in_specs=(P(None, LEAF, None), P(None, COL, LEAF), P(None, LEAF, COL), P()),
        out_specs=P(None, LEAF, None),
        check_vma=False,
    )
```

```python
import jax
import jax.numpy as jnp
import numpy as np
from jax import lax
from jax.sharding import Mesh, PartitionSpec as P

level_starts = (0, 16, 24, 28, 30)
level_counts = (16, 8, 4, 2, 1)
LEAF = ("x", "y")
COL = ("z", "core")


def pair_offset(tree_level):
    initial_position = 0
    for lower in range(tree_level):
        initial_position = initial_position + level_counts[lower] * (4 - lower)
    return initial_position


def climb_table(parent):
    climbed = [jnp.arange(parent.shape[0], dtype=jnp.int32)]
    for distance in range(4):
        climbed.append(jnp.take(parent, climbed[-1]))
    return climbed


def level_onehot(climbed, source_level, distance):
    start, count = level_starts[source_level], level_counts[source_level]
    target = source_level + distance
    anc = climbed[distance][start : start + count]
    slots = jnp.arange(level_counts[target], dtype=jnp.int32) + level_starts[target]
    return (slots[:, None] == anc[None, :]).astype(jnp.float32)


def pair_slice(panel_local, source_level, distance):
    start = pair_offset(source_level) + distance - 1
    stride = 4 - source_level
    stop = pair_offset(source_level) + level_counts[source_level] * stride
    return panel_local[start:stop:stride]


def xor_perm(n, bit):
    return [(i, i ^ bit) for i in range(n)]


def a2a_allreduce(x, axis, n):
    shape = x.shape
    k = shape[0]
    if k >= n:
        pieces = x.reshape((n, k // n) + shape[1:])
    else:
        rows = shape[1] * k // n
        pieces = x.reshape((n, 1, rows) + shape[2:])
    got = lax.all_to_all(pieces, axis, 0, 0, tiled=False)
    owned = jnp.sum(got.astype(jnp.float32), axis=0).astype(jnp.bfloat16)
    spread = lax.all_to_all(jnp.broadcast_to(owned[None], (n,) + owned.shape), axis, 0, 0, tiled=False)
    return spread.reshape(shape)


def doubling_allreduce(x, axis, n):
    bit = 1
    while bit < n:
        x = (x.astype(jnp.float32) + lax.ppermute(x, axis, xor_perm(n, bit)).astype(jnp.float32)).astype(jnp.bfloat16)
        bit *= 2
    return x


def staged_allreduce(x, stages):
    shape = x.shape
    total = 1
    for _, size in stages:
        total *= size
    cur = x.reshape((total, shape[0] // total) + shape[1:])
    for axis, size in stages:
        pieces = cur.reshape((size, cur.shape[0] // size) + cur.shape[1:])
        got = lax.all_to_all(pieces, axis, 0, 0, tiled=False)
        cur = jnp.sum(got.astype(jnp.float32), axis=0).astype(jnp.bfloat16)
    for axis, size in reversed(stages):
        spread = lax.all_to_all(jnp.broadcast_to(cur[None], (size,) + cur.shape), axis, 0, 0, tiled=False)
        cur = spread.reshape((size * cur.shape[0],) + cur.shape[1:])
    return cur.reshape(shape)


def group_allreduce(x, axis, n):
    small = 1 if axis == LEAF else 4
    if x.shape[0] <= small:
        return doubling_allreduce(x, axis, n)
    if axis == COL and x.shape[0] >= 2 * n:
        return staged_allreduce(x, (("core", 2), ("z", 4)))
    return a2a_allreduce(x, axis, n)


def solve(right_side, diag_local, panel_local, parent):
    climbed = climb_table(parent)
    n_leaf = 16
    n_col = 8
    forward_levels = [None] * 5
    forward_half = [None] * 5
    for tree_level in range(5):
        start_node = level_starts[tree_level]
        node_count = level_counts[tree_level]
        reduced = right_side[start_node : start_node + node_count]
        if tree_level > 0:
            partial_value = None
            for source_level in range(tree_level):
                distance = tree_level - source_level
                products = jnp.einsum(
                    "sjv,svk->sjk",
                    pair_slice(panel_local, source_level, distance),
                    forward_half[source_level],
                    preferred_element_type=jnp.float32,
                )
                onehot = level_onehot(climbed, source_level, distance)
                term = jnp.sum(
                    jnp.where(onehot[:, :, None, None] > 0, products[None], 0.0), axis=1
                )
                partial_value = term if partial_value is None else partial_value + term
            reduced = reduced - group_allreduce(
                partial_value.astype(jnp.bfloat16), COL, n_col
            ).astype(jnp.float32)
        division_count = jnp.einsum(
            "kcl,klr->kcr",
            diag_local[start_node : start_node + node_count],
            reduced.astype(jnp.bfloat16),
            preferred_element_type=jnp.float32,
        )
        forward_value = group_allreduce(
            division_count.astype(jnp.bfloat16), LEAF, n_leaf
        )
        forward_levels[tree_level] = forward_value.astype(jnp.float32)
        forward_half[tree_level] = forward_value
    solution_half = [None] * 5
    results = [None] * 5
    for tree_level in (4, 3, 2, 1, 0):
        start_node = level_starts[tree_level]
        node_count = level_counts[tree_level]
        corrected = forward_levels[tree_level]
        if tree_level < 4:
            partial_value = None
            for distance in range(1, 5 - tree_level):
                onehot = level_onehot(climbed, tree_level, distance)
                upper_node = jnp.einsum(
                    "ks,kjr->sjr",
                    onehot,
                    solution_half[tree_level + distance].astype(jnp.float32),
                    precision=lax.Precision.HIGHEST,
                ).astype(jnp.bfloat16)
                term = jnp.einsum(
                    "boj,boh->bjh",
                    pair_slice(panel_local, tree_level, distance),
                    upper_node,
                    preferred_element_type=jnp.float32,
                )
                partial_value = term if partial_value is None else partial_value + term
            corrected = corrected - group_allreduce(
                partial_value.astype(jnp.bfloat16), LEAF, n_leaf
            ).astype(jnp.float32)
        division_count = jnp.einsum(
            "kcl,kcr->klr",
            diag_local[start_node : start_node + node_count],
            corrected.astype(jnp.bfloat16),
            preferred_element_type=jnp.float32,
        )
        solution = group_allreduce(division_count.astype(jnp.bfloat16), COL, n_col)
        results[tree_level] = solution.astype(jnp.float32)
        solution_half[tree_level] = solution
    return jnp.concatenate(results, axis=0)


def solution(mesh):
    chips = Mesh(mesh.devices.reshape(4, 4, 4, 2), ("x", "y", "z", "core"))
    return jax.shard_map(
        solve,
        mesh=chips,
        in_specs=(P(None, LEAF, None), P(None, COL, LEAF), P(None, LEAF, COL), P()),
        out_specs=P(None, LEAF, None),
        check_vma=False,
    )
```

```python
import jax
import jax.numpy as jnp
import numpy as np
from jax import lax
from jax.sharding import Mesh, PartitionSpec as P

level_starts = (0, 16, 24, 28, 30)
level_counts = (16, 8, 4, 2, 1)
LEAF = ("x", "y")
COL = ("z", "core")


def pair_offset(tree_level):
    initial_position = 0
    for lower in range(tree_level):
        initial_position = initial_position + level_counts[lower] * (4 - lower)
    return initial_position


def climb_table(parent):
    climbed = [jnp.arange(parent.shape[0], dtype=jnp.int32)]
    for distance in range(4):
        climbed.append(jnp.take(parent, climbed[-1]))
    return climbed


def level_onehot(climbed, source_level, distance):
    start, count = level_starts[source_level], level_counts[source_level]
    target = source_level + distance
    anc = climbed[distance][start : start + count]
    slots = jnp.arange(level_counts[target], dtype=jnp.int32) + level_starts[target]
    return (slots[:, None] == anc[None, :]).astype(jnp.float32)


def pair_slice(panel_local, source_level, distance):
    start = pair_offset(source_level) + distance - 1
    stride = 4 - source_level
    stop = pair_offset(source_level) + level_counts[source_level] * stride
    return panel_local[start:stop:stride]


def xor_perm(n, bit):
    return [(i, i ^ bit) for i in range(n)]


def a2a_allreduce(x, axis, n):
    shape = x.shape
    k = shape[0]
    if k >= n:
        pieces = x.reshape((n, k // n) + shape[1:])
    else:
        rows = shape[1] * k // n
        pieces = x.reshape((n, 1, rows) + shape[2:])
    got = lax.all_to_all(pieces, axis, 0, 0, tiled=False)
    owned = jnp.sum(got.astype(jnp.float32), axis=0).astype(jnp.bfloat16)
    spread = lax.all_to_all(jnp.broadcast_to(owned[None], (n,) + owned.shape), axis, 0, 0, tiled=False)
    return spread.reshape(shape)


def doubling_allreduce(x, axis, n):
    bit = 1
    while bit < n:
        x = (x.astype(jnp.float32) + lax.ppermute(x, axis, xor_perm(n, bit)).astype(jnp.float32)).astype(jnp.bfloat16)
        bit *= 2
    return x


def staged_allreduce(x, stages):
    shape = x.shape
    total = 1
    for _, size in stages:
        total *= size
    cur = x.reshape((total, shape[0] // total) + shape[1:])
    for axis, size in stages:
        pieces = cur.reshape((size, cur.shape[0] // size) + cur.shape[1:])
        got = lax.all_to_all(pieces, axis, 0, 0, tiled=False)
        cur = jnp.sum(got.astype(jnp.float32), axis=0).astype(jnp.bfloat16)
    for axis, size in reversed(stages):
        spread = lax.all_to_all(jnp.broadcast_to(cur[None], (size,) + cur.shape), axis, 0, 0, tiled=False)
        cur = spread.reshape((size * cur.shape[0],) + cur.shape[1:])
    return cur.reshape(shape)


def group_allreduce(x, axis, n):
    small = 1 if axis == LEAF else 4
    if x.shape[0] <= small:
        return doubling_allreduce(x, axis, n)
    if axis == COL and x.shape[0] >= 2 * n:
        return staged_allreduce(x, (("core", 2), ("z", 4)))
    return a2a_allreduce(x, axis, n)


def solve(right_side, diag_local, panel_local, parent):
    climbed = climb_table(parent)
    n_leaf = 16
    n_col = 8
    forward_levels = [None] * 5
    forward_half = [None] * 5
    for tree_level in range(5):
        start_node = level_starts[tree_level]
        node_count = level_counts[tree_level]
        reduced = right_side[start_node : start_node + node_count]
        if tree_level > 0:
            partial_value = None
            for source_level in range(tree_level):
                distance = tree_level - source_level
                products = jnp.einsum(
                    "sjv,svk->sjk",
                    pair_slice(panel_local, source_level, distance),
                    forward_half[source_level],
                    preferred_element_type=jnp.float32,
                )
                onehot = level_onehot(climbed, source_level, distance)
                term = jnp.sum(
                    jnp.where(onehot[:, :, None, None] > 0, products[None], 0.0), axis=1
                )
                partial_value = term if partial_value is None else partial_value + term
            reduced = reduced - group_allreduce(
                partial_value.astype(jnp.bfloat16), COL, n_col
            ).astype(jnp.float32)
        division_count = jnp.einsum(
            "kcl,klr->kcr",
            diag_local[start_node : start_node + node_count],
            reduced.astype(jnp.bfloat16),
            preferred_element_type=jnp.float32,
        )
        forward_value = group_allreduce(
            division_count.astype(jnp.bfloat16), LEAF, n_leaf
        )
        forward_levels[tree_level] = forward_value.astype(jnp.float32)
        forward_half[tree_level] = forward_value
    solution_half = [None] * 5
    results = [None] * 5
    for tree_level in (4, 3, 2, 1, 0):
        start_node = level_starts[tree_level]
        node_count = level_counts[tree_level]
        corrected = forward_levels[tree_level]
        if tree_level < 4:
            partial_value = None
            for distance in range(1, 5 - tree_level):
                onehot = level_onehot(climbed, tree_level, distance)
                upper_node = jnp.sum(
                    jnp.where(
                        onehot[:, :, None, None] > 0,
                        solution_half[tree_level + distance].astype(jnp.float32)[:, None],
                        0.0,
                    ),
                    axis=0,
                ).astype(jnp.bfloat16)
                term = jnp.einsum(
                    "boj,boh->bjh",
                    pair_slice(panel_local, tree_level, distance),
                    upper_node,
                    preferred_element_type=jnp.float32,
                )
                partial_value = term if partial_value is None else partial_value + term
            corrected = corrected - group_allreduce(
                partial_value.astype(jnp.bfloat16), LEAF, n_leaf
            ).astype(jnp.float32)
        division_count = jnp.einsum(
            "kcl,kcr->klr",
            diag_local[start_node : start_node + node_count],
            corrected.astype(jnp.bfloat16),
            preferred_element_type=jnp.float32,
        )
        solution = group_allreduce(division_count.astype(jnp.bfloat16), COL, n_col)
        results[tree_level] = solution.astype(jnp.float32)
        solution_half[tree_level] = solution
    return jnp.concatenate(results, axis=0)


def solution(mesh):
    chips = Mesh(mesh.devices.reshape(4, 4, 4, 2), ("x", "y", "z", "core"))
    return jax.shard_map(
        solve,
        mesh=chips,
        in_specs=(P(None, LEAF, None), P(None, COL, LEAF), P(None, LEAF, COL), P()),
        out_specs=P(None, LEAF, None),
        check_vma=False,
    )
```

```python
import jax
import jax.numpy as jnp
import numpy as np
from jax import lax
from jax.sharding import Mesh, PartitionSpec as P

level_starts = (0, 16, 24, 28, 30)
level_counts = (16, 8, 4, 2, 1)
LEAF = ("x", "y")
COL = ("z", "core")


def pair_offset(tree_level):
    initial_position = 0
    for lower in range(tree_level):
        initial_position = initial_position + level_counts[lower] * (4 - lower)
    return initial_position


def climb_table(parent):
    climbed = [jnp.arange(parent.shape[0], dtype=jnp.int32)]
    for distance in range(4):
        climbed.append(jnp.take(parent, climbed[-1]))
    return climbed


def level_onehot(climbed, source_level, distance):
    start, count = level_starts[source_level], level_counts[source_level]
    target = source_level + distance
    anc = climbed[distance][start : start + count]
    slots = jnp.arange(level_counts[target], dtype=jnp.int32) + level_starts[target]
    return (slots[:, None] == anc[None, :]).astype(jnp.float32)


def pair_slice(panel_local, source_level, distance):
    start = pair_offset(source_level) + distance - 1
    stride = 4 - source_level
    stop = pair_offset(source_level) + level_counts[source_level] * stride
    return panel_local[start:stop:stride]


def xor_perm(n, bit):
    return [(i, i ^ bit) for i in range(n)]


def a2a_allreduce(x, axis, n):
    shape = x.shape
    k = shape[0]
    if k >= n:
        pieces = x.reshape((n, k // n) + shape[1:])
    else:
        rows = shape[1] * k // n
        pieces = x.reshape((n, 1, rows) + shape[2:])
    got = lax.all_to_all(pieces, axis, 0, 0, tiled=False)
    owned = jnp.sum(got.astype(jnp.float32), axis=0).astype(jnp.bfloat16)
    spread = lax.all_to_all(jnp.broadcast_to(owned[None], (n,) + owned.shape), axis, 0, 0, tiled=False)
    return spread.reshape(shape)


def doubling_allreduce(x, axis, n):
    bit = 1
    while bit < n:
        x = (x.astype(jnp.float32) + lax.ppermute(x, axis, xor_perm(n, bit)).astype(jnp.float32)).astype(jnp.bfloat16)
        bit *= 2
    return x


def staged_allreduce(x, stages):
    shape = x.shape
    total = 1
    for _, size in stages:
        total *= size
    cur = x.reshape((total, shape[0] // total) + shape[1:])
    for axis, size in stages:
        pieces = cur.reshape((size, cur.shape[0] // size) + cur.shape[1:])
        got = lax.all_to_all(pieces, axis, 0, 0, tiled=False)
        cur = jnp.sum(got.astype(jnp.float32), axis=0).astype(jnp.bfloat16)
    for axis, size in reversed(stages):
        spread = lax.all_to_all(jnp.broadcast_to(cur[None], (size,) + cur.shape), axis, 0, 0, tiled=False)
        cur = spread.reshape((size * cur.shape[0],) + cur.shape[1:])
    return cur.reshape(shape)


def group_allreduce(x, axis, n):
    small = 1 if axis == LEAF else 4
    if x.shape[0] <= small:
        return doubling_allreduce(x, axis, n)
    if axis == COL and x.shape[0] >= 2 * n:
        return staged_allreduce(x, (("core", 2), ("z", 4)))
    return a2a_allreduce(x, axis, n)


def solve(right_side, diag_local, panel_local, parent):
    climbed = climb_table(parent)
    n_leaf = 16
    n_col = 8
    forward_levels = [None] * 5
    forward_half = [None] * 5
    for tree_level in range(5):
        start_node = level_starts[tree_level]
        node_count = level_counts[tree_level]
        reduced = right_side[start_node : start_node + node_count]
        if tree_level > 0:
            partial_value = None
            for source_level in range(tree_level):
                distance = tree_level - source_level
                products = jnp.einsum(
                    "sjv,svk->sjk",
                    pair_slice(panel_local, source_level, distance),
                    forward_half[source_level],
                    preferred_element_type=jnp.float32,
                )
                onehot = level_onehot(climbed, source_level, distance)
                term = jnp.sum(
                    jnp.where(onehot[:, :, None, None] > 0, products[None], 0.0), axis=1
                )
                partial_value = term if partial_value is None else partial_value + term
            reduced = reduced - group_allreduce(
                partial_value.astype(jnp.bfloat16), COL, n_col
            ).astype(jnp.float32)
        division_count = jnp.einsum(
            "kcl,klr->kcr",
            diag_local[start_node : start_node + node_count],
            reduced.astype(jnp.bfloat16),
            preferred_element_type=jnp.float32,
        )
        forward_value = group_allreduce(
            division_count.astype(jnp.bfloat16), LEAF, n_leaf
        )
        forward_levels[tree_level] = forward_value.astype(jnp.float32)
        forward_half[tree_level] = forward_value
    solution_half = [None] * 5
    results = [None] * 5
    for tree_level in (4, 3, 2, 1, 0):
        start_node = level_starts[tree_level]
        node_count = level_counts[tree_level]
        corrected = forward_levels[tree_level]
        if tree_level < 4:
            partial_value = None
            for distance in range(1, 5 - tree_level):
                onehot = level_onehot(climbed, tree_level, distance)
                upper_node = jnp.einsum(
                    "ks,kjr->sjr",
                    onehot.astype(jnp.bfloat16),
                    solution_half[tree_level + distance],
                    preferred_element_type=jnp.float32,
                ).astype(jnp.bfloat16)
                term = jnp.einsum(
                    "boj,boh->bjh",
                    pair_slice(panel_local, tree_level, distance),
                    upper_node,
                    preferred_element_type=jnp.float32,
                )
                partial_value = term if partial_value is None else partial_value + term
            corrected = corrected - group_allreduce(
                partial_value.astype(jnp.bfloat16), LEAF, n_leaf
            ).astype(jnp.float32)
        division_count = jnp.einsum(
            "kcl,kcr->klr",
            diag_local[start_node : start_node + node_count],
            corrected.astype(jnp.bfloat16),
            preferred_element_type=jnp.float32,
        )
        solution = group_allreduce(division_count.astype(jnp.bfloat16), COL, n_col)
        results[tree_level] = solution.astype(jnp.float32)
        solution_half[tree_level] = solution
    return jnp.concatenate(results, axis=0)


def solution(mesh):
    chips = Mesh(mesh.devices.reshape(4, 4, 4, 2), ("x", "y", "z", "core"))
    return jax.shard_map(
        solve,
        mesh=chips,
        in_specs=(P(None, LEAF, None), P(None, COL, LEAF), P(None, LEAF, COL), P()),
        out_specs=P(None, LEAF, None),
        check_vma=False,
    )
```

```python
import jax
import jax.numpy as jnp
import numpy as np
from jax import lax
from jax.sharding import Mesh, PartitionSpec as P

level_starts = (0, 16, 24, 28, 30)
level_counts = (16, 8, 4, 2, 1)
LEAF = ("x", "y")
COL = ("z", "core")


def pair_offset(tree_level):
    initial_position = 0
    for lower in range(tree_level):
        initial_position = initial_position + level_counts[lower] * (4 - lower)
    return initial_position


def climb_table(parent):
    climbed = [jnp.arange(parent.shape[0], dtype=jnp.int32)]
    for distance in range(4):
        climbed.append(jnp.take(parent, climbed[-1]))
    return climbed


def level_onehot(climbed, source_level, distance):
    start, count = level_starts[source_level], level_counts[source_level]
    target = source_level + distance
    anc = climbed[distance][start : start + count]
    slots = jnp.arange(level_counts[target], dtype=jnp.int32) + level_starts[target]
    return (slots[:, None] == anc[None, :]).astype(jnp.float32)


def pair_slice(panel_local, source_level, distance):
    start = pair_offset(source_level) + distance - 1
    stride = 4 - source_level
    stop = pair_offset(source_level) + level_counts[source_level] * stride
    return panel_local[start:stop:stride]


def xor_perm(n, bit):
    return [(i, i ^ bit) for i in range(n)]


def a2a_allreduce(x, axis, n):
    shape = x.shape
    k = shape[0]
    if k >= n:
        pieces = x.reshape((n, k // n) + shape[1:])
    else:
        rows = shape[1] * k // n
        pieces = x.reshape((n, 1, rows) + shape[2:])
    got = lax.all_to_all(pieces, axis, 0, 0, tiled=False)
    if got.size * n <= (1 << 22):
        copies = jnp.broadcast_to(got.astype(jnp.float32)[None], (n,) + got.shape)
        sent = jnp.sum(copies, axis=1).astype(jnp.bfloat16)
    else:
        owned = jnp.sum(got.astype(jnp.float32), axis=0).astype(jnp.bfloat16)
        sent = jnp.broadcast_to(owned[None], (n,) + owned.shape)
    spread = lax.all_to_all(sent, axis, 0, 0, tiled=False)
    return spread.reshape(shape)


def doubling_allreduce(x, axis, n):
    bit = 1
    while bit < n:
        x = (x.astype(jnp.float32) + lax.ppermute(x, axis, xor_perm(n, bit)).astype(jnp.float32)).astype(jnp.bfloat16)
        bit *= 2
    return x


def staged_allreduce(x, stages):
    shape = x.shape
    total = 1
    for _, size in stages:
        total *= size
    cur = x.reshape((total, shape[0] // total) + shape[1:])
    for axis, size in stages:
        pieces = cur.reshape((size, cur.shape[0] // size) + cur.shape[1:])
        got = lax.all_to_all(pieces, axis, 0, 0, tiled=False)
        cur = jnp.sum(got.astype(jnp.float32), axis=0).astype(jnp.bfloat16)
    for axis, size in reversed(stages):
        spread = lax.all_to_all(jnp.broadcast_to(cur[None], (size,) + cur.shape), axis, 0, 0, tiled=False)
        cur = spread.reshape((size * cur.shape[0],) + cur.shape[1:])
    return cur.reshape(shape)


def group_allreduce(x, axis, n):
    small = 1 if axis == LEAF else 4
    if x.shape[0] <= small:
        return doubling_allreduce(x, axis, n)
    if axis == COL and x.shape[0] >= 2 * n:
        return staged_allreduce(x, (("core", 2), ("z", 4)))
    return a2a_allreduce(x, axis, n)


def solve(right_side, diag_local, panel_local, parent):
    climbed = climb_table(parent)
    n_leaf = 16
    n_col = 8
    forward_levels = [None] * 5
    forward_half = [None] * 5
    for tree_level in range(5):
        start_node = level_starts[tree_level]
        node_count = level_counts[tree_level]
        reduced = right_side[start_node : start_node + node_count]
        if tree_level > 0:
            partial_value = None
            for source_level in range(tree_level):
                distance = tree_level - source_level
                products = jnp.einsum(
                    "sjv,svk->sjk",
                    pair_slice(panel_local, source_level, distance),
                    forward_half[source_level],
                    preferred_element_type=jnp.float32,
                )
                onehot = level_onehot(climbed, source_level, distance)
                term = jnp.sum(
                    jnp.where(onehot[:, :, None, None] > 0, products[None], 0.0), axis=1
                )
                partial_value = term if partial_value is None else partial_value + term
            reduced = reduced - group_allreduce(
                partial_value.astype(jnp.bfloat16), COL, n_col
            ).astype(jnp.float32)
        division_count = jnp.einsum(
            "kcl,klr->kcr",
            diag_local[start_node : start_node + node_count],
            reduced.astype(jnp.bfloat16),
            preferred_element_type=jnp.float32,
        )
        forward_value = group_allreduce(
            division_count.astype(jnp.bfloat16), LEAF, n_leaf
        )
        forward_levels[tree_level] = forward_value.astype(jnp.float32)
        forward_half[tree_level] = forward_value
    solution_half = [None] * 5
    results = [None] * 5
    for tree_level in (4, 3, 2, 1, 0):
        start_node = level_starts[tree_level]
        node_count = level_counts[tree_level]
        corrected = forward_levels[tree_level]
        if tree_level < 4:
            partial_value = None
            for distance in range(1, 5 - tree_level):
                onehot = level_onehot(climbed, tree_level, distance)
                upper_node = jnp.einsum(
                    "ks,kjr->sjr",
                    onehot.astype(jnp.bfloat16),
                    solution_half[tree_level + distance],
                    preferred_element_type=jnp.float32,
                ).astype(jnp.bfloat16)
                term = jnp.einsum(
                    "boj,boh->bjh",
                    pair_slice(panel_local, tree_level, distance),
                    upper_node,
                    preferred_element_type=jnp.float32,
                )
                partial_value = term if partial_value is None else partial_value + term
            corrected = corrected - group_allreduce(
                partial_value.astype(jnp.bfloat16), LEAF, n_leaf
            ).astype(jnp.float32)
        division_count = jnp.einsum(
            "kcl,kcr->klr",
            diag_local[start_node : start_node + node_count],
            corrected.astype(jnp.bfloat16),
            preferred_element_type=jnp.float32,
        )
        solution = group_allreduce(division_count.astype(jnp.bfloat16), COL, n_col)
        results[tree_level] = solution.astype(jnp.float32)
        solution_half[tree_level] = solution
    return jnp.concatenate(results, axis=0)


def solution(mesh):
    chips = Mesh(mesh.devices.reshape(4, 4, 4, 2), ("x", "y", "z", "core"))
    return jax.shard_map(
        solve,
        mesh=chips,
        in_specs=(P(None, LEAF, None), P(None, COL, LEAF), P(None, LEAF, COL), P()),
        out_specs=P(None, LEAF, None),
        check_vma=False,
    )
```

```python
import jax
import jax.numpy as jnp
import numpy as np
from jax import lax
from jax.sharding import Mesh, PartitionSpec as P

level_starts = (0, 16, 24, 28, 30)
level_counts = (16, 8, 4, 2, 1)
LEAF = ("x", "y")
COL = ("z", "core")


def pair_offset(tree_level):
    initial_position = 0
    for lower in range(tree_level):
        initial_position = initial_position + level_counts[lower] * (4 - lower)
    return initial_position


def climb_table(parent):
    climbed = [jnp.arange(parent.shape[0], dtype=jnp.int32)]
    for distance in range(4):
        climbed.append(jnp.take(parent, climbed[-1]))
    return climbed


def level_onehot(climbed, source_level, distance):
    start, count = level_starts[source_level], level_counts[source_level]
    target = source_level + distance
    anc = climbed[distance][start : start + count]
    slots = jnp.arange(level_counts[target], dtype=jnp.int32) + level_starts[target]
    return (slots[:, None] == anc[None, :]).astype(jnp.float32)


def pair_slice(panel_local, source_level, distance):
    start = pair_offset(source_level) + distance - 1
    stride = 4 - source_level
    stop = pair_offset(source_level) + level_counts[source_level] * stride
    return panel_local[start:stop:stride]


def xor_perm(n, bit):
    return [(i, i ^ bit) for i in range(n)]


def a2a_allreduce(x, axis, n):
    shape = x.shape
    k = shape[0]
    if k >= n:
        pieces = x.reshape((n, k // n) + shape[1:])
    else:
        rows = shape[1] * k // n
        pieces = x.reshape((n, 1, rows) + shape[2:])
    got = lax.all_to_all(pieces, axis, 0, 0, tiled=False)
    if got.size * n <= (1 << 22):
        copies = jnp.broadcast_to(got.astype(jnp.float32)[None], (n,) + got.shape)
        sent = jnp.sum(copies, axis=1).astype(jnp.bfloat16)
    else:
        owned = jnp.sum(got.astype(jnp.float32), axis=0).astype(jnp.bfloat16)
        sent = jnp.broadcast_to(owned[None], (n,) + owned.shape)
    spread = lax.all_to_all(sent, axis, 0, 0, tiled=False)
    return spread.reshape(shape)


def doubling_allreduce(x, axis, n):
    bit = 1
    while bit < n:
        x = (x.astype(jnp.float32) + lax.ppermute(x, axis, xor_perm(n, bit)).astype(jnp.float32)).astype(jnp.bfloat16)
        bit *= 2
    return x


def staged_allreduce(x, stages):
    shape = x.shape
    total = 1
    for _, size in stages:
        total *= size
    cur = x.reshape((total, shape[0] // total) + shape[1:])
    for axis, size in stages:
        pieces = cur.reshape((size, cur.shape[0] // size) + cur.shape[1:])
        got = lax.all_to_all(pieces, axis, 0, 0, tiled=False)
        cur = jnp.sum(got.astype(jnp.float32), axis=0).astype(jnp.bfloat16)
    for axis, size in reversed(stages):
        spread = lax.all_to_all(jnp.broadcast_to(cur[None], (size,) + cur.shape), axis, 0, 0, tiled=False)
        cur = spread.reshape((size * cur.shape[0],) + cur.shape[1:])
    return cur.reshape(shape)


def group_allreduce(x, axis, n):
    small = 1 if axis == LEAF else 4
    if x.shape[0] <= small:
        return doubling_allreduce(x, axis, n)
    if axis == COL and x.shape[0] >= 2 * n:
        return staged_allreduce(x, (("core", 2), ("z", 4)))
    return a2a_allreduce(x, axis, n)


def solve(right_side, diag_local, panel_local, parent):
    climbed = climb_table(parent)
    n_leaf = 16
    n_col = 8
    forward_levels = [None] * 5
    forward_half = [None] * 5
    for tree_level in range(5):
        start_node = level_starts[tree_level]
        node_count = level_counts[tree_level]
        reduced = right_side[start_node : start_node + node_count]
        if tree_level > 0:
            partial_value = None
            for source_level in range(tree_level):
                distance = tree_level - source_level
                products = jnp.einsum(
                    "sjv,svk->sjk",
                    pair_slice(panel_local, source_level, distance),
                    forward_half[source_level],
                    preferred_element_type=jnp.float32,
                )
                onehot = level_onehot(climbed, source_level, distance)
                term = jnp.sum(
                    jnp.where(onehot[:, :, None, None] > 0, products[None], 0.0), axis=1
                )
                partial_value = term if partial_value is None else partial_value + term
            reduced = reduced - group_allreduce(
                partial_value.astype(jnp.bfloat16), COL, n_col
            ).astype(jnp.float32)
        division_count = jnp.einsum(
            "kcl,klr->kcr",
            diag_local[start_node : start_node + node_count],
            reduced.astype(jnp.bfloat16),
            preferred_element_type=jnp.float32,
        )
        forward_value = group_allreduce(
            division_count.astype(jnp.bfloat16), LEAF, n_leaf
        )
        forward_levels[tree_level] = forward_value.astype(jnp.float32)
        forward_half[tree_level] = forward_value
    solution_half = [None] * 5
    results = jnp.zeros(right_side.shape, jnp.float32)
    for tree_level in (4, 3, 2, 1, 0):
        start_node = level_starts[tree_level]
        node_count = level_counts[tree_level]
        corrected = forward_levels[tree_level]
        if tree_level < 4:
            partial_value = None
            for distance in range(1, 5 - tree_level):
                onehot = level_onehot(climbed, tree_level, distance)
                upper_node = jnp.einsum(
                    "ks,kjr->sjr",
                    onehot.astype(jnp.bfloat16),
                    solution_half[tree_level + distance],
                    preferred_element_type=jnp.float32,
                ).astype(jnp.bfloat16)
                term = jnp.einsum(
                    "boj,boh->bjh",
                    pair_slice(panel_local, tree_level, distance),
                    upper_node,
                    preferred_element_type=jnp.float32,
                )
                partial_value = term if partial_value is None else partial_value + term
            corrected = corrected - group_allreduce(
                partial_value.astype(jnp.bfloat16), LEAF, n_leaf
            ).astype(jnp.float32)
        division_count = jnp.einsum(
            "kcl,kcr->klr",
            diag_local[start_node : start_node + node_count],
            corrected.astype(jnp.bfloat16),
            preferred_element_type=jnp.float32,
        )
        solution = group_allreduce(division_count.astype(jnp.bfloat16), COL, n_col)
        results = lax.dynamic_update_slice_in_dim(results, solution.astype(jnp.float32), start_node, axis=0)
        solution_half[tree_level] = solution
    return results


def solution(mesh):
    chips = Mesh(mesh.devices.reshape(4, 4, 4, 2), ("x", "y", "z", "core"))
    return jax.shard_map(
        solve,
        mesh=chips,
        in_specs=(P(None, LEAF, None), P(None, COL, LEAF), P(None, LEAF, COL), P()),
        out_specs=P(None, LEAF, None),
        check_vma=False,
    )
```
